256 devices in a mesh: segment: 4 (over y), rows: 64 (over x, z, core).
Axes of the slice: x: 4, y: 4, z: 8, core: 2. Of those that a mesh axis runs over, the one named last changes fastest.
Arguments:
- clip: bfloat16 [2, 2, 256, 64, 128], P(None, None, 'rows'), may hold values from -6 to 6
- weights: bfloat16 [4, 3456, 128], P('segment'), may hold values from -0.109375 to 0.109375
- cotangent: bfloat16 [2, 2, 256, 64, 128], P(None, None, 'rows'), may hold values from -0.0234375 to 0.0234375
Outputs:
- weight_grads: float32 [4, 3456, 128], P('segment')
The draws below stay inside these ranges and needn't reach their ends.
All inputs are finite; a program needn't handle non-finite values.
Results may differ from the reference program's by a relative error of at most 0.007.
Values may be sent and summed in bfloat16 or wider, within the bound.
No kernel may reach another device: no remote copies, remote signals or barrier semaphores. Data moves between devices by JAX's collectives and lax.ppermute only.
A program may use at most 128 MiB of HBM per device.

```python
import jax
import jax.numpy as jnp
from jax import lax

CHANNELS = 128
FRAMES = 2
MICRO = 2
COLS = 64
SEGMENTS = 4
HEIGHT = 256
POSITIONS = 65536


def levels(key, extent, split, least, largest):
    gain, own = 1.0, jax.random.fold_in(key, 6)
    for dim, parts in split:
        steps = jnp.exp(jax.random.uniform(jax.random.fold_in(own, dim), (parts,), jnp.float32, least / len(split), largest / len(split)))
        gain = gain * jnp.repeat(steps, extent[dim] // parts).reshape([-1 if axis == dim else 1 for axis in range(len(extent))])
    return gain


def bell_draw(key, dims, scale, limit, cuts=(), kind=jnp.bfloat16):
    drawn = jax.random.normal(key, dims, jnp.float32) * scale
    if len(cuts) > 0:
        drawn = levels(key, dims, cuts, -0.22, 0.18) * drawn
    return jnp.clip(drawn, min=-limit, max=limit).astype(kind)


def setup_inputs(seed: int = 0) -> dict:
    streams_of = jax.random.split(jax.random.key(seed), 4)
    clip = bell_draw(streams_of[0], (MICRO, FRAMES, HEIGHT, COLS, CHANNELS), 1.0, 6.0, ((2, 64),))
    weights = bell_draw(streams_of[1], (SEGMENTS, 27 * CHANNELS, CHANNELS), (27 * CHANNELS) ** -0.5, 0.109375, ((0, 4),))
    cotangent = bell_draw(streams_of[2], (MICRO, FRAMES, HEIGHT, COLS, CHANNELS), POSITIONS ** -0.5, 0.0234375, ((2, 64),))
    return dict(clip=clip, weights=weights, cotangent=cotangent)


def patches(padded, flipped):
    frame_count = padded.shape[0] - 2
    row_count = padded.shape[1] - 2
    col_count = padded.shape[2] - 2
    pieces = []
    for lag_t in range(3):
        for lag_h in range(3):
            for lag_w in range(3):
                if flipped:
                    start_t, start_h, start_w = 2 - lag_t, 2 - lag_h, 2 - lag_w
                else:
                    start_t, start_h, start_w = lag_t, lag_h, lag_w
                pieces.append(padded[start_t:start_t + frame_count, start_h:start_h + row_count, start_w:start_w + col_count])
    joined = jnp.concatenate(pieces, axis=-1)
    return joined.reshape(frame_count * row_count * col_count, joined.shape[-1])


def slope(pre_act):
    sigma = jax.nn.sigmoid(pre_act)
    return sigma * (1.0 + pre_act * (1.0 - sigma))


def reference(clip, weights, cotangent):
    channels = clip.shape[-1]
    grads = [jnp.zeros((27 * channels, channels), jnp.float32) for segment_no in range(SEGMENTS)]
    for batch_no in range(MICRO):
        current = clip[batch_no]
        shape_four = current.shape
        saved = []
        for segment_no in range(SEGMENTS):
            padded = jnp.pad(current, ((2, 0), (1, 1), (1, 1), (0, 0)))
            pre_act = jnp.dot(patches(padded, False), weights[segment_no], preferred_element_type=jnp.float32)
            saved.append((padded, pre_act))
            current = (current.reshape(-1, channels).astype(jnp.float32) + jax.nn.silu(pre_act)).astype(jnp.bfloat16).reshape(shape_four)
        upstream = cotangent[batch_no]
        for segment_no in reversed(range(SEGMENTS)):
            padded, pre_act = saved[segment_no]
            delta = (upstream.reshape(-1, channels).astype(jnp.float32) * slope(pre_act)).astype(jnp.bfloat16)
            grads[segment_no] = grads[segment_no] + lax.dot_general(patches(padded, False), delta, (((0,), (0,)), ((), ())), preferred_element_type=jnp.float32)
            delta_pad = jnp.pad(delta.reshape(shape_four), ((0, 2), (1, 1), (1, 1), (0, 0)))
            flipped_w = weights[segment_no].reshape(27, channels, channels).transpose(0, 2, 1).reshape(27 * channels, channels)
            back = jnp.dot(patches(delta_pad, True), flipped_w, preferred_element_type=jnp.float32)
            upstream = (upstream.reshape(-1, channels).astype(jnp.float32) + back).astype(jnp.bfloat16).reshape(shape_four)
    return jnp.stack(grads)
```

```python
import jax
import jax.numpy as jnp
from jax import lax
from jax.sharding import PartitionSpec as P

AXES = ("segment", "rows")


def shifted(x, segment_count, row_count, seg_from, seg_to, row_step):
    pairs = []
    for i in range(row_count):
        j = i + row_step
        if 0 <= j < row_count:
            pairs.append((seg_from * row_count + i, seg_to * row_count + j))
    return lax.ppermute(x, AXES, pairs)


def widened(x, segment_count, row_count, seg_from, seg_to, width):
    rows = x.shape[2]
    if seg_from == seg_to:
        mid = x
    else:
        mid = shifted(x, segment_count, row_count, seg_from, seg_to, 0)
    above = shifted(x[:, :, rows - width :], segment_count, row_count, seg_from, seg_to, 1)
    below = shifted(x[:, :, :width], segment_count, row_count, seg_from, seg_to, -1)
    return jnp.concatenate([above, mid, below], axis=2)


def forward_conv(x_ext, kernel5):
    return lax.conv_general_dilated(
        x_ext,
        kernel5,
        window_strides=(1, 1, 1),
        padding=((2, 0), (0, 0), (1, 1)),
        dimension_numbers=("NDHWC", "DHWIO", "NDHWC"),
        preferred_element_type=jnp.float32,
    )


def back_conv(delta_ext, flipped5):
    return lax.conv_general_dilated(
        delta_ext,
        flipped5,
        window_strides=(1, 1, 1),
        padding=((0, 2), (0, 0), (1, 1)),
        dimension_numbers=("NDHWC", "DHWIO", "NDHWC"),
        preferred_element_type=jnp.float32,
    )


def kernel_grad(x_ext, delta):
    padded = jnp.pad(x_ext, ((0, 0), (2, 0), (0, 0), (1, 1), (0, 0)))
    return lax.conv_general_dilated(
        padded,
        delta,
        window_strides=(1, 1, 1),
        padding="VALID",
        dimension_numbers=("CDHWN", "IDHWO", "DHWNC"),
        preferred_element_type=jnp.float32,
    )


def slope(pre_act):
    sigma = jax.nn.sigmoid(pre_act)
    return sigma * (1.0 + pre_act * (1.0 - sigma))


def tree_sum(x, axis, count):
    index = lax.axis_index(axis)
    steps = count.bit_length() - 1
    buf = x
    for k in range(steps):
        bit = (index >> k) & 1
        half = buf.shape[0] // 2
        low, high = buf[:half], buf[half:]
        keep = jnp.where(bit == 0, low, high)
        send = jnp.where(bit == 0, high, low)
        got = lax.ppermute(send, axis, [(j, j ^ (1 << k)) for j in range(count)])
        buf = keep + got
    for k in reversed(range(steps)):
        bit = (index >> k) & 1
        got = lax.ppermute(buf, axis, [(j, j ^ (1 << k)) for j in range(count)])
        buf = jnp.where(bit == 0, jnp.concatenate([buf, got]), jnp.concatenate([got, buf]))
    return buf


def per_device(clip, weights, cotangent):
    segment_count = lax.axis_size("segment")
    row_count = lax.axis_size("rows")
    segment_no = lax.axis_index("segment")
    channels = clip.shape[-1]
    kernel5 = weights[0].reshape(3, 3, 3, channels, channels)
    flipped5 = kernel5[::-1, ::-1, ::-1].transpose(0, 1, 2, 4, 3)

    received = widened(clip, segment_count, row_count, 0, 0, 2)
    saved = []
    for s in range(segment_count):
        x_ext = received
        pre_act = forward_conv(x_ext, kernel5)
        core = x_ext[:, :, 2:-2]
        output = (core.astype(jnp.float32) + jax.nn.silu(pre_act[:, :, 1:-1])).astype(jnp.bfloat16)
        saved.append((x_ext, pre_act))
        if s + 1 < segment_count:
            received = widened(output, segment_count, row_count, s, s + 1, 2)

    last = segment_count - 1
    upstream = widened(cotangent, segment_count, row_count, last, last, 1)
    grad_total = jnp.zeros((27 * channels, channels), jnp.float32)
    for s in reversed(range(segment_count)):
        x_ext, pre_act = saved[s]
        delta = (upstream.astype(jnp.float32) * slope(pre_act)).astype(jnp.bfloat16)
        grad = kernel_grad(x_ext[:, :, 1:-1], delta[:, :, 1:-1]).reshape(27 * channels, channels)
        grad_total = jnp.where(segment_no == s, grad, grad_total)
        if s > 0:
            back = back_conv(delta, flipped5)
            gradient = (upstream[:, :, 1:-1].astype(jnp.float32) + back).astype(jnp.bfloat16)
            upstream = widened(gradient, segment_count, row_count, s, s - 1, 1)

    summed = tree_sum(grad_total, "rows", row_count)
    return summed[None]


def solution(mesh):
    in_specs = (
        P(None, None, "rows", None, None),
        P("segment", None, None),
        P(None, None, "rows", None, None),
    )
    out_specs = P("segment", None, None)
    return jax.shard_map(
        per_device, mesh=mesh, in_specs=in_specs, out_specs=out_specs, check_vma=False
    )
```

```python
import jax
import jax.numpy as jnp
from jax import lax
from jax.sharding import PartitionSpec as P

AXES = ("segment", "rows")


def shifted(x, segment_count, row_count, seg_from, seg_to, row_step):
    pairs = []
    for i in range(row_count):
        j = i + row_step
        if 0 <= j < row_count:
            pairs.append((seg_from * row_count + i, seg_to * row_count + j))
    return lax.ppermute(x, AXES, pairs)


def widened(x, segment_count, row_count, seg_from, seg_to, width):
    rows = x.shape[2]
    if seg_from == seg_to:
        mid = x
    else:
        mid = shifted(x, segment_count, row_count, seg_from, seg_to, 0)
    above = shifted(x[:, :, rows - width :], segment_count, row_count, seg_from, seg_to, 1)
    below = shifted(x[:, :, :width], segment_count, row_count, seg_from, seg_to, -1)
    return jnp.concatenate([above, mid, below], axis=2)


def forward_conv(x_ext, kernel5):
    return lax.conv_general_dilated(
        x_ext,
        kernel5,
        window_strides=(1, 1, 1),
        padding=((2, 0), (0, 0), (1, 1)),
        dimension_numbers=("NDHWC", "DHWIO", "NDHWC"),
        preferred_element_type=jnp.float32,
    )


def back_conv(delta_ext, flipped5):
    return lax.conv_general_dilated(
        delta_ext,
        flipped5,
        window_strides=(1, 1, 1),
        padding=((0, 2), (0, 0), (1, 1)),
        dimension_numbers=("NDHWC", "DHWIO", "NDHWC"),
        preferred_element_type=jnp.float32,
    )


def kernel_grad(x_ext, delta):
    padded = jnp.pad(x_ext, ((0, 0), (2, 0), (0, 0), (1, 1), (0, 0)))
    return lax.conv_general_dilated(
        padded,
        delta,
        window_strides=(1, 1, 1),
        padding="VALID",
        dimension_numbers=("CDHWN", "IDHWO", "DHWNC"),
        preferred_element_type=jnp.float32,
    )


def slope(pre_act):
    sigma = jax.nn.sigmoid(pre_act)
    return sigma * (1.0 + pre_act * (1.0 - sigma))


def tree_sum(x, axis, count):
    index = lax.axis_index(axis)
    steps = count.bit_length() - 1
    buf = x
    for k in range(steps):
        bit = (index >> k) & 1
        half = buf.shape[0] // 2
        low, high = buf[:half], buf[half:]
        keep = jnp.where(bit == 0, low, high)
        send = jnp.where(bit == 0, high, low).astype(jnp.bfloat16)
        got = lax.ppermute(send, axis, [(j, j ^ (1 << k)) for j in range(count)])
        buf = keep + got.astype(jnp.float32)
    buf = buf.astype(jnp.bfloat16)
    for k in reversed(range(steps)):
        bit = (index >> k) & 1
        got = lax.ppermute(buf, axis, [(j, j ^ (1 << k)) for j in range(count)])
        buf = jnp.where(bit == 0, jnp.concatenate([buf, got]), jnp.concatenate([got, buf]))
    return buf.astype(jnp.float32)


def per_device(clip, weights, cotangent):
    segment_count = lax.axis_size("segment")
    row_count = lax.axis_size("rows")
    segment_no = lax.axis_index("segment")
    channels = clip.shape[-1]
    kernel5 = weights[0].reshape(3, 3, 3, channels, channels)
    flipped5 = kernel5[::-1, ::-1, ::-1].transpose(0, 1, 2, 4, 3)

    received = widened(clip, segment_count, row_count, 0, 0, 2)
    saved = []
    for s in range(segment_count):
        x_ext = received

        def forward_tick(x_ext):
            pre_act = forward_conv(x_ext, kernel5)
            core = x_ext[:, :, 2:-2].astype(jnp.float32)
            output = (core + jax.nn.silu(pre_act[:, :, 1:-1])).astype(jnp.bfloat16)
            return pre_act, output

        def forward_idle(x_ext):
            pre_act = jnp.zeros(x_ext.shape[:2] + (x_ext.shape[2] - 2,) + x_ext.shape[3:], jnp.float32)
            return pre_act, jnp.zeros_like(x_ext[:, :, 2:-2])

        pre_act, output = lax.cond(segment_no == s, forward_tick, forward_idle, x_ext)
        saved.append((x_ext, pre_act))
        if s + 1 < segment_count:
            received = widened(output, segment_count, row_count, s, s + 1, 2)

    last = segment_count - 1
    upstream = widened(cotangent, segment_count, row_count, last, last, 1)
    grad_total = jnp.zeros((27 * channels, channels), jnp.float32)
    for s in reversed(range(segment_count)):
        x_ext, pre_act = saved[s]

        def backward_tick(upstream, pre_act):
            delta = (upstream.astype(jnp.float32) * slope(pre_act)).astype(jnp.bfloat16)
            if s == 0:
                return delta, upstream[:, :, 1:-1]
            back = back_conv(delta, flipped5)
            gradient = (upstream[:, :, 1:-1].astype(jnp.float32) + back).astype(jnp.bfloat16)
            return delta, gradient

        def backward_idle(upstream, pre_act):
            return jnp.zeros_like(upstream), jnp.zeros_like(upstream[:, :, 1:-1])

        delta, gradient = lax.cond(segment_no == s, backward_tick, backward_idle, upstream, pre_act)
        if s > 0:
            upstream = widened(gradient, segment_count, row_count, s, s - 1, 1)

        def grad_tick(x_ext, delta, grad_total):
            return kernel_grad(x_ext[:, :, 1:-1], delta[:, :, 1:-1]).reshape(27 * channels, channels)

        def grad_idle(x_ext, delta, grad_total):
            return grad_total

        grad_total = lax.cond(segment_no == s, grad_tick, grad_idle, x_ext, delta, grad_total)

    summed = tree_sum(grad_total, "rows", row_count)
    return summed[None]


def solution(mesh):
    in_specs = (
        P(None, None, "rows", None, None),
        P("segment", None, None),
        P(None, None, "rows", None, None),
    )
    out_specs = P("segment", None, None)
    return jax.shard_map(
        per_device, mesh=mesh, in_specs=in_specs, out_specs=out_specs, check_vma=False
    )
```

```python
import jax
import jax.numpy as jnp
from jax import lax
from jax.sharding import PartitionSpec as P

AXES = ("segment", "rows")


def shifted(x, segment_count, row_count, seg_from, seg_to, row_step):
    pairs = []
    for i in range(row_count):
        j = i + row_step
        if 0 <= j < row_count:
            pairs.append((seg_from * row_count + i, seg_to * row_count + j))
    return lax.ppermute(x, AXES, pairs)


def widened(x, segment_count, row_count, seg_from, seg_to, width):
    rows = x.shape[2]
    if seg_from == seg_to:
        mid = x
    else:
        mid = shifted(x, segment_count, row_count, seg_from, seg_to, 0)
    above = shifted(x[:, :, rows - width :], segment_count, row_count, seg_from, seg_to, 1)
    below = shifted(x[:, :, :width], segment_count, row_count, seg_from, seg_to, -1)
    return jnp.concatenate([above, mid, below], axis=2)


def forward_conv(x_ext, kernel5):
    return lax.conv_general_dilated(
        x_ext,
        kernel5,
        window_strides=(1, 1, 1),
        padding=((2, 0), (0, 0), (1, 1)),
        dimension_numbers=("NDHWC", "DHWIO", "NDHWC"),
        preferred_element_type=jnp.float32,
    )


def back_conv(delta_ext, flipped5):
    return lax.conv_general_dilated(
        delta_ext,
        flipped5,
        window_strides=(1, 1, 1),
        padding=((0, 2), (0, 0), (1, 1)),
        dimension_numbers=("NDHWC", "DHWIO", "NDHWC"),
        preferred_element_type=jnp.float32,
    )


def kernel_grad(x_ext, delta):
    padded = jnp.pad(x_ext, ((0, 0), (2, 0), (0, 0), (1, 1), (0, 0)))
    return lax.conv_general_dilated(
        padded,
        delta,
        window_strides=(1, 1, 1),
        padding="VALID",
        dimension_numbers=("CDHWN", "IDHWO", "DHWNC"),
        preferred_element_type=jnp.float32,
    )


def slope(pre_act):
    sigma = jax.nn.sigmoid(pre_act)
    return sigma * (1.0 + pre_act * (1.0 - sigma))


def pick(parts, index):
    out = parts[0]
    for k in range(1, len(parts)):
        out = jnp.where(index == k, parts[k], out)
    return out


def digit_pairs(count, stride, radix, step):
    pairs = []
    for j in range(count):
        digit = (j // stride) % radix
        pairs.append((j, j + ((digit + step) % radix - digit) * stride))
    return pairs


def tree_sum(x, axis, count, digits):
    index = lax.axis_index(axis)
    buf = x
    for stride, radix in digits:
        digit = (index // stride) % radix
        size = buf.shape[0] // radix
        parts = [buf[k * size : (k + 1) * size] for k in range(radix)]
        acc = pick(parts, digit)
        for step in range(1, radix):
            send = pick(parts, (digit + step) % radix).astype(jnp.bfloat16)
            got = lax.ppermute(send, axis, digit_pairs(count, stride, radix, step))
            acc = acc + got.astype(jnp.float32)
        buf = acc
    buf = buf.astype(jnp.bfloat16)
    for stride, radix in reversed(digits):
        digit = (index // stride) % radix
        gots = [buf]
        for step in range(1, radix):
            gots.append(lax.ppermute(buf, axis, digit_pairs(count, stride, radix, step)))
        buf = jnp.concatenate([pick(gots, (digit - k) % radix) for k in range(radix)])
    return buf.astype(jnp.float32)


def digits_of(count):
    if count == 64:
        return [(1, 2), (16, 4), (2, 2), (4, 4)]
    digits = []
    stride = 1
    while stride < count:
        digits.append((stride, 2))
        stride *= 2
    return digits


def per_device(clip, weights, cotangent):
    segment_count = lax.axis_size("segment")
    row_count = lax.axis_size("rows")
    segment_no = lax.axis_index("segment")
    channels = clip.shape[-1]
    kernel5 = weights[0].reshape(3, 3, 3, channels, channels)
    flipped5 = kernel5[::-1, ::-1, ::-1].transpose(0, 1, 2, 4, 3)

    rows = clip.shape[2]
    above = lax.ppermute(
        jnp.concatenate([clip[:, :, rows - 2 :], cotangent[:, :, rows - 1 :]], axis=2),
        "rows", [(i, i + 1) for i in range(row_count - 1)],
    )
    below = lax.ppermute(
        jnp.concatenate([clip[:, :, :2], cotangent[:, :, :1]], axis=2),
        "rows", [(i + 1, i) for i in range(row_count - 1)],
    )
    received = jnp.concatenate([above[:, :, :2], clip, below[:, :, :2]], axis=2)
    cot_ext = jnp.concatenate([above[:, :, 2:], cotangent, below[:, :, 2:]], axis=2)
    saved = []
    for s in range(segment_count):
        x_ext = received

        def forward_tick(x_ext):
            pre_act = forward_conv(x_ext, kernel5)
            core = x_ext[:, :, 2:-2].astype(jnp.float32)
            output = (core + jax.nn.silu(pre_act[:, :, 1:-1])).astype(jnp.bfloat16)
            return pre_act, output

        def forward_idle(x_ext):
            pre_act = jnp.zeros(x_ext.shape[:2] + (x_ext.shape[2] - 2,) + x_ext.shape[3:], jnp.float32)
            return pre_act, jnp.zeros_like(x_ext[:, :, 2:-2])

        pre_act, output = lax.cond(segment_no == s, forward_tick, forward_idle, x_ext)
        saved.append((x_ext, pre_act))
        if s + 1 < segment_count:
            received = widened(output, segment_count, row_count, s, s + 1, 2)

    last = segment_count - 1
    upstream = cot_ext
    grad_total = jnp.zeros((27 * channels, channels), jnp.float32)
    for s in reversed(range(segment_count)):
        x_ext, pre_act = saved[s]

        def backward_tick(upstream, pre_act):
            delta = (upstream.astype(jnp.float32) * slope(pre_act)).astype(jnp.bfloat16)
            if s == 0:
                return delta, upstream[:, :, 1:-1]
            back = back_conv(delta, flipped5)
            gradient = (upstream[:, :, 1:-1].astype(jnp.float32) + back).astype(jnp.bfloat16)
            return delta, gradient

        def backward_idle(upstream, pre_act):
            return jnp.zeros_like(upstream), jnp.zeros_like(upstream[:, :, 1:-1])

        delta, gradient = lax.cond(segment_no == s, backward_tick, backward_idle, upstream, pre_act)
        if s > 0:
            upstream = widened(gradient, segment_count, row_count, s, s - 1, 1)

        def grad_tick(x_ext, delta, grad_total):
            return kernel_grad(x_ext[:, :, 1:-1], delta[:, :, 1:-1]).reshape(27 * channels, channels)

        def grad_idle(x_ext, delta, grad_total):
            return grad_total

        grad_total = lax.cond(segment_no == s, grad_tick, grad_idle, x_ext, delta, grad_total)

    summed = tree_sum(grad_total, "rows", row_count, digits_of(row_count))
    return summed[None]


def solution(mesh):
    in_specs = (
        P(None, None, "rows", None, None),
        P("segment", None, None),
        P(None, None, "rows", None, None),
    )
    out_specs = P("segment", None, None)
    return jax.shard_map(
        per_device, mesh=mesh, in_specs=in_specs, out_specs=out_specs, check_vma=False
    )
```

```python
import jax
import jax.numpy as jnp
from jax import lax
from jax.sharding import PartitionSpec as P

AXES = ("segment", "rows")


def shifted(x, segment_count, row_count, seg_from, seg_to, row_step):
    pairs = []
    for i in range(row_count):
        j = i + row_step
        if 0 <= j < row_count:
            pairs.append((seg_from * row_count + i, seg_to * row_count + j))
    return lax.ppermute(x, AXES, pairs)


def widened(x, segment_count, row_count, seg_from, seg_to, width):
    rows = x.shape[2]
    if seg_from == seg_to:
        mid = x
    else:
        mid = shifted(x, segment_count, row_count, seg_from, seg_to, 0)
    above = shifted(x[:, :, rows - width :], segment_count, row_count, seg_from, seg_to, 1)
    below = shifted(x[:, :, :width], segment_count, row_count, seg_from, seg_to, -1)
    return jnp.concatenate([above, mid, below], axis=2)


def forward_conv(x_ext, kernel5):
    return lax.conv_general_dilated(
        x_ext,
        kernel5,
        window_strides=(1, 1, 1),
        padding=((2, 0), (0, 0), (1, 1)),
        dimension_numbers=("NDHWC", "DHWIO", "NDHWC"),
        preferred_element_type=jnp.float32,
    )


def back_conv(delta_ext, flipped5):
    return lax.conv_general_dilated(
        delta_ext,
        flipped5,
        window_strides=(1, 1, 1),
        padding=((0, 2), (0, 0), (1, 1)),
        dimension_numbers=("NDHWC", "DHWIO", "NDHWC"),
        preferred_element_type=jnp.float32,
    )


def kernel_grad(x_ext, delta):
    padded = jnp.pad(x_ext, ((0, 0), (2, 0), (0, 0), (1, 1), (0, 0)))
    return lax.conv_general_dilated(
        padded,
        delta,
        window_strides=(1, 1, 1),
        padding="VALID",
        dimension_numbers=("CDHWN", "IDHWO", "DHWNC"),
        preferred_element_type=jnp.float32,
    )


def slope(pre_act):
    sigma = jax.nn.sigmoid(pre_act)
    return sigma * (1.0 + pre_act * (1.0 - sigma))


def pick(parts, index):
    out = parts[0]
    for k in range(1, len(parts)):
        out = jnp.where(index == k, parts[k], out)
    return out


def digit_pairs(count, stride, radix, step):
    pairs = []
    for j in range(count):
        digit = (j // stride) % radix
        pairs.append((j, j + ((digit + step) % radix - digit) * stride))
    return pairs


def tree_sum(x, axis, count, digits):
    index = lax.axis_index(axis)
    buf = x
    for stride, radix in digits:
        digit = (index // stride) % radix
        size = buf.shape[0] // radix
        parts = [buf[k * size : (k + 1) * size] for k in range(radix)]
        acc = pick(parts, digit)
        for step in range(1, radix):
            send = pick(parts, (digit + step) % radix).astype(jnp.bfloat16)
            got = lax.ppermute(send, axis, digit_pairs(count, stride, radix, step))
            acc = acc + got.astype(jnp.float32)
        buf = acc
    buf = buf.astype(jnp.bfloat16)
    for stride, radix in reversed(digits):
        digit = (index // stride) % radix
        gots = [buf]
        for step in range(1, radix):
            gots.append(lax.ppermute(buf, axis, digit_pairs(count, stride, radix, step)))
        buf = jnp.concatenate([pick(gots, (digit - k) % radix) for k in range(radix)])
    return buf.astype(jnp.float32)


def digits_of(count):
    if count == 64:
        return [(1, 2), (16, 4), (2, 2), (4, 4)]
    digits = []
    stride = 1
    while stride < count:
        digits.append((stride, 2))
        stride *= 2
    return digits


def per_device(clip, weights, cotangent):
    segment_count = lax.axis_size("segment")
    row_count = lax.axis_size("rows")
    segment_no = lax.axis_index("segment")
    channels = clip.shape[-1]
    kernel5 = weights[0].reshape(3, 3, 3, channels, channels)
    flipped5 = kernel5[::-1, ::-1, ::-1].transpose(0, 1, 2, 4, 3)

    rows = clip.shape[2]
    width = segment_count + 1
    reach = -(-width // rows)
    above_parts, below_parts = [], []
    cot_above = cot_below = None
    for dist in range(1, reach + 1):
        take = min(rows, width - (dist - 1) * rows)
        up = clip[:, :, rows - take :]
        down = clip[:, :, :take]
        if dist == 1:
            up = jnp.concatenate([up, cotangent[:, :, rows - 1 :]], axis=2)
            down = jnp.concatenate([down, cotangent[:, :, :1]], axis=2)
        up = lax.ppermute(up, "rows", [(i, i + dist) for i in range(row_count - dist)])
        down = lax.ppermute(down, "rows", [(i + dist, i) for i in range(row_count - dist)])
        if dist == 1:
            cot_above, cot_below = up[:, :, take:], down[:, :, take:]
            up, down = up[:, :, :take], down[:, :, :take]
        above_parts.insert(0, up)
        below_parts.append(down)
    received = jnp.concatenate(above_parts + [clip] + below_parts, axis=2)
    cot_ext = jnp.concatenate([cot_above, cotangent, cot_below], axis=2)
    row_no = lax.axis_index("rows")
    saved = []
    for s in range(segment_count):
        x_ext = received
        ghost = width - s - 1
        first = row_no * rows - ghost
        absolute = first + jnp.arange(rows + 2 * ghost)
        inside = ((absolute >= 0) & (absolute < row_count * rows))[None, None, :, None, None]

        def forward_tick(x_ext):
            pre_act = forward_conv(x_ext, kernel5)
            core = x_ext[:, :, 1:-1].astype(jnp.float32)
            output = (core + jax.nn.silu(pre_act)).astype(jnp.bfloat16)
            return pre_act, jnp.where(inside, output, jnp.zeros_like(output))

        def forward_idle(x_ext):
            pre_act = jnp.zeros(x_ext.shape[:2] + (x_ext.shape[2] - 2,) + x_ext.shape[3:], jnp.float32)
            return pre_act, jnp.zeros_like(x_ext[:, :, 1:-1])

        pre_act, output = lax.cond(segment_no == s, forward_tick, forward_idle, x_ext)
        keep_x = width - s - 2
        keep_p = width - s - 2
        saved.append((x_ext[:, :, keep_x : keep_x + rows + 4], pre_act[:, :, keep_p : keep_p + rows + 2]))
        if s + 1 < segment_count:
            received = shifted(output, segment_count, row_count, s, s + 1, 0)

    last = segment_count - 1
    upstream = cot_ext
    grad_total = jnp.zeros((27 * channels, channels), jnp.float32)
    for s in reversed(range(segment_count)):
        x_ext, pre_act = saved[s]

        def backward_tick(upstream, pre_act):
            delta = (upstream.astype(jnp.float32) * slope(pre_act)).astype(jnp.bfloat16)
            if s == 0:
                return delta, upstream[:, :, 1:-1]
            back = back_conv(delta, flipped5)
            gradient = (upstream[:, :, 1:-1].astype(jnp.float32) + back).astype(jnp.bfloat16)
            return delta, gradient

        def backward_idle(upstream, pre_act):
            return jnp.zeros_like(upstream), jnp.zeros_like(upstream[:, :, 1:-1])

        delta, gradient = lax.cond(segment_no == s, backward_tick, backward_idle, upstream, pre_act)
        if s > 0:
            upstream = widened(gradient, segment_count, row_count, s, s - 1, 1)

        def grad_tick(x_ext, delta, grad_total):
            return kernel_grad(x_ext[:, :, 1:-1], delta[:, :, 1:-1]).reshape(27 * channels, channels)

        def grad_idle(x_ext, delta, grad_total):
            return grad_total

        grad_total = lax.cond(segment_no == s, grad_tick, grad_idle, x_ext, delta, grad_total)

    summed = tree_sum(grad_total, "rows", row_count, digits_of(row_count))
    return summed[None]


def solution(mesh):
    in_specs = (
        P(None, None, "rows", None, None),
        P("segment", None, None),
        P(None, None, "rows", None, None),
    )
    out_specs = P("segment", None, None)
    return jax.shard_map(
        per_device, mesh=mesh, in_specs=in_specs, out_specs=out_specs, check_vma=False
    )
```

```python
import jax
import jax.numpy as jnp
from jax import lax
from jax.sharding import PartitionSpec as P

AXES = ("segment", "rows")


def shifted(x, segment_count, row_count, seg_from, seg_to, row_step):
    pairs = []
    for i in range(row_count):
        j = i + row_step
        if 0 <= j < row_count:
            pairs.append((seg_from * row_count + i, seg_to * row_count + j))
    return lax.ppermute(x, AXES, pairs)


def widened(x, segment_count, row_count, seg_from, seg_to, width):
    rows = x.shape[2]
    if seg_from == seg_to:
        mid = x
    else:
        mid = shifted(x, segment_count, row_count, seg_from, seg_to, 0)
    above = shifted(x[:, :, rows - width :], segment_count, row_count, seg_from, seg_to, 1)
    below = shifted(x[:, :, :width], segment_count, row_count, seg_from, seg_to, -1)
    return jnp.concatenate([above, mid, below], axis=2)


def forward_conv(x_ext, kernel5):
    return lax.conv_general_dilated(
        x_ext,
        kernel5,
        window_strides=(1, 1, 1),
        padding=((2, 0), (0, 0), (1, 1)),
        dimension_numbers=("NDHWC", "DHWIO", "NDHWC"),
        preferred_element_type=jnp.float32,
    )


def back_conv(delta_ext, flipped5):
    return lax.conv_general_dilated(
        delta_ext,
        flipped5,
        window_strides=(1, 1, 1),
        padding=((0, 2), (0, 0), (1, 1)),
        dimension_numbers=("NDHWC", "DHWIO", "NDHWC"),
        preferred_element_type=jnp.float32,
    )


def kernel_grad(x_ext, delta):
    padded = jnp.pad(x_ext, ((0, 0), (2, 0), (0, 0), (1, 1), (0, 0)))
    return lax.conv_general_dilated(
        padded,
        delta,
        window_strides=(1, 1, 1),
        padding="VALID",
        dimension_numbers=("CDHWN", "IDHWO", "DHWNC"),
        preferred_element_type=jnp.float32,
    )


def slope(pre_act):
    sigma = jax.nn.sigmoid(pre_act)
    return sigma * (1.0 + pre_act * (1.0 - sigma))


def pick(parts, index):
    out = parts[0]
    for k in range(1, len(parts)):
        out = jnp.where(index == k, parts[k], out)
    return out


def digit_pairs(count, stride, radix, step):
    pairs = []
    for j in range(count):
        digit = (j // stride) % radix
        pairs.append((j, j + ((digit + step) % radix - digit) * stride))
    return pairs


def tree_sum(x, axis, count, digits):
    index = lax.axis_index(axis)
    buf = x
    for stride, radix in digits:
        digit = (index // stride) % radix
        size = buf.shape[0] // radix
        parts = [buf[k * size : (k + 1) * size] for k in range(radix)]
        acc = pick(parts, digit)
        for step in range(1, radix):
            send = pick(parts, (digit + step) % radix).astype(jnp.bfloat16)
            got = lax.ppermute(send, axis, digit_pairs(count, stride, radix, step))
            acc = acc + got.astype(jnp.float32)
        buf = acc
    buf = buf.astype(jnp.bfloat16)
    for stride, radix in reversed(digits):
        digit = (index // stride) % radix
        gots = [buf]
        for step in range(1, radix):
            gots.append(lax.ppermute(buf, axis, digit_pairs(count, stride, radix, step)))
        buf = jnp.concatenate([pick(gots, (digit - k) % radix) for k in range(radix)])
    return buf.astype(jnp.float32)


def digits_of(count):
    if count == 64:
        return [(1, 2), (16, 4), (2, 2), (4, 4)]
    digits = []
    stride = 1
    while stride < count:
        digits.append((stride, 2))
        stride *= 2
    return digits


def per_device(clip, weights, cotangent):
    segment_count = lax.axis_size("segment")
    row_count = lax.axis_size("rows")
    segment_no = lax.axis_index("segment")
    channels = clip.shape[-1]
    kernel5 = weights[0].reshape(3, 3, 3, channels, channels)
    flipped5 = kernel5[::-1, ::-1, ::-1].transpose(0, 1, 2, 4, 3)

    rows = clip.shape[2]
    above = lax.ppermute(
        jnp.concatenate([clip[:, :, rows - 2 :], cotangent[:, :, rows - 1 :]], axis=2),
        "rows", [(i, i + 1) for i in range(row_count - 1)],
    )
    below = lax.ppermute(
        jnp.concatenate([clip[:, :, :2], cotangent[:, :, :1]], axis=2),
        "rows", [(i + 1, i) for i in range(row_count - 1)],
    )
    received = jnp.concatenate([above[:, :, :2], clip, below[:, :, :2]], axis=2)
    cot_ext = jnp.concatenate([above[:, :, 2:], cotangent, below[:, :, 2:]], axis=2)
    micro_count = clip.shape[0]
    received = [received[m : m + 1] for m in range(micro_count)]
    saved = []
    for s in range(segment_count):
        saved.append([])
        for m in range(micro_count):
            x_ext = received[m]

            def forward_tick(x_ext):
                pre_act = forward_conv(x_ext, kernel5)
                core = x_ext[:, :, 2:-2].astype(jnp.float32)
                output = (core + jax.nn.silu(pre_act[:, :, 1:-1])).astype(jnp.bfloat16)
                return pre_act, output

            def forward_idle(x_ext):
                pre_act = jnp.zeros(x_ext.shape[:2] + (x_ext.shape[2] - 2,) + x_ext.shape[3:], jnp.float32)
                return pre_act, jnp.zeros_like(x_ext[:, :, 2:-2])

            pre_act, output = lax.cond(segment_no == s, forward_tick, forward_idle, x_ext)
            saved[s].append((x_ext, pre_act))
            if s + 1 < segment_count:
                received[m] = widened(output, segment_count, row_count, s, s + 1, 2)

    upstream = [cot_ext[m : m + 1] for m in range(micro_count)]
    grad_total = jnp.zeros((27 * channels, channels), jnp.float32)
    for s in reversed(range(segment_count)):
        for m in range(micro_count):
            x_ext, pre_act = saved[s][m]

            def backward_tick(upstream, pre_act):
                delta = (upstream.astype(jnp.float32) * slope(pre_act)).astype(jnp.bfloat16)
                if s == 0:
                    return delta, upstream[:, :, 1:-1]
                back = back_conv(delta, flipped5)
                gradient = (upstream[:, :, 1:-1].astype(jnp.float32) + back).astype(jnp.bfloat16)
                return delta, gradient

            def backward_idle(upstream, pre_act):
                return jnp.zeros_like(upstream), jnp.zeros_like(upstream[:, :, 1:-1])

            delta, gradient = lax.cond(segment_no == s, backward_tick, backward_idle, upstream[m], pre_act)
            if s > 0:
                upstream[m] = widened(gradient, segment_count, row_count, s, s - 1, 1)

            def grad_tick(x_ext, delta, grad_total):
                grad = kernel_grad(x_ext[:, :, 1:-1], delta[:, :, 1:-1])
                return grad_total + grad.reshape(27 * channels, channels)

            def grad_idle(x_ext, delta, grad_total):
                return grad_total

            grad_total = lax.cond(segment_no == s, grad_tick, grad_idle, x_ext, delta, grad_total)

    summed = tree_sum(grad_total, "rows", row_count, digits_of(row_count))
    return summed[None]


def solution(mesh):
    in_specs = (
        P(None, None, "rows", None, None),
        P("segment", None, None),
        P(None, None, "rows", None, None),
    )
    out_specs = P("segment", None, None)
    return jax.shard_map(
        per_device, mesh=mesh, in_specs=in_specs, out_specs=out_specs, check_vma=False
    )
```

```python
import jax
import jax.numpy as jnp
from jax import lax
from jax.sharding import PartitionSpec as P

AXES = ("segment", "rows")


def shifted(x, segment_count, row_count, seg_from, seg_to, row_step):
    pairs = []
    for i in range(row_count):
        j = i + row_step
        if 0 <= j < row_count:
            pairs.append((seg_from * row_count + i, seg_to * row_count + j))
    return lax.ppermute(x, AXES, pairs)


def widened(x, segment_count, row_count, seg_from, seg_to, width):
    rows = x.shape[2]
    mid = shifted(x, segment_count, row_count, seg_from, seg_to, 0)
    above = shifted(mid[:, :, rows - width :], segment_count, row_count, seg_to, seg_to, 1)
    below = shifted(mid[:, :, :width], segment_count, row_count, seg_to, seg_to, -1)
    return jnp.concatenate([above, mid, below], axis=2)


def forward_conv(x_ext, kernel5):
    return lax.conv_general_dilated(
        x_ext,
        kernel5,
        window_strides=(1, 1, 1),
        padding=((2, 0), (0, 0), (1, 1)),
        dimension_numbers=("NDHWC", "DHWIO", "NDHWC"),
        preferred_element_type=jnp.float32,
    )


def back_conv(delta_ext, flipped5):
    return lax.conv_general_dilated(
        delta_ext,
        flipped5,
        window_strides=(1, 1, 1),
        padding=((0, 2), (0, 0), (1, 1)),
        dimension_numbers=("NDHWC", "DHWIO", "NDHWC"),
        preferred_element_type=jnp.float32,
    )


def kernel_grad(x_ext, delta):
    padded = jnp.pad(x_ext, ((0, 0), (2, 0), (0, 0), (1, 1), (0, 0)))
    return lax.conv_general_dilated(
        padded,
        delta,
        window_strides=(1, 1, 1),
        padding="VALID",
        dimension_numbers=("CDHWN", "IDHWO", "DHWNC"),
        preferred_element_type=jnp.float32,
    )


def slope(pre_act):
    sigma = jax.nn.sigmoid(pre_act)
    return sigma * (1.0 + pre_act * (1.0 - sigma))


def pick(parts, index):
    out = parts[0]
    for k in range(1, len(parts)):
        out = jnp.where(index == k, parts[k], out)
    return out


def digit_pairs(count, stride, radix, step):
    pairs = []
    for j in range(count):
        digit = (j // stride) % radix
        pairs.append((j, j + ((digit + step) % radix - digit) * stride))
    return pairs


def tree_sum(x, axis, count, digits):
    index = lax.axis_index(axis)
    buf = x
    for stride, radix in digits:
        digit = (index // stride) % radix
        size = buf.shape[0] // radix
        parts = [buf[k * size : (k + 1) * size] for k in range(radix)]
        acc = pick(parts, digit)
        for step in range(1, radix):
            send = pick(parts, (digit + step) % radix).astype(jnp.bfloat16)
            got = lax.ppermute(send, axis, digit_pairs(count, stride, radix, step))
            acc = acc + got.astype(jnp.float32)
        buf = acc
    buf = buf.astype(jnp.bfloat16)
    for stride, radix in reversed(digits):
        digit = (index // stride) % radix
        gots = [buf]
        for step in range(1, radix):
            gots.append(lax.ppermute(buf, axis, digit_pairs(count, stride, radix, step)))
        buf = jnp.concatenate([pick(gots, (digit - k) % radix) for k in range(radix)])
    return buf.astype(jnp.float32)


def digits_of(count):
    if count == 64:
        return [(1, 2), (16, 4), (2, 2), (4, 4)]
    digits = []
    stride = 1
    while stride < count:
        digits.append((stride, 2))
        stride *= 2
    return digits


def per_device(clip, weights, cotangent):
    segment_count = lax.axis_size("segment")
    row_count = lax.axis_size("rows")
    segment_no = lax.axis_index("segment")
    channels = clip.shape[-1]
    kernel5 = weights[0].reshape(3, 3, 3, channels, channels)
    flipped5 = kernel5[::-1, ::-1, ::-1].transpose(0, 1, 2, 4, 3)

    rows = clip.shape[2]
    above = lax.ppermute(
        jnp.concatenate([clip[:, :, rows - 2 :], cotangent[:, :, rows - 1 :]], axis=2),
        "rows", [(i, i + 1) for i in range(row_count - 1)],
    )
    below = lax.ppermute(
        jnp.concatenate([clip[:, :, :2], cotangent[:, :, :1]], axis=2),
        "rows", [(i + 1, i) for i in range(row_count - 1)],
    )
    received = jnp.concatenate([above[:, :, :2], clip, below[:, :, :2]], axis=2)
    cot_ext = jnp.concatenate([above[:, :, 2:], cotangent, below[:, :, 2:]], axis=2)
    saved = []
    for s in range(segment_count):
        x_ext = received

        def forward_tick(x_ext):
            pre_act = forward_conv(x_ext, kernel5)
            core = x_ext[:, :, 2:-2].astype(jnp.float32)
            output = (core + jax.nn.silu(pre_act[:, :, 1:-1])).astype(jnp.bfloat16)
            return pre_act, output

        def forward_idle(x_ext):
            pre_act = jnp.zeros(x_ext.shape[:2] + (x_ext.shape[2] - 2,) + x_ext.shape[3:], jnp.float32)
            return pre_act, jnp.zeros_like(x_ext[:, :, 2:-2])

        pre_act, output = lax.cond(segment_no == s, forward_tick, forward_idle, x_ext)
        saved.append((x_ext, pre_act))
        if s + 1 < segment_count:
            received = widened(output, segment_count, row_count, s, s + 1, 2)

    last = segment_count - 1
    upstream = cot_ext
    grad_total = jnp.zeros((27 * channels, channels), jnp.float32)
    for s in reversed(range(segment_count)):
        x_ext, pre_act = saved[s]

        def backward_tick(upstream, pre_act):
            delta = (upstream.astype(jnp.float32) * slope(pre_act)).astype(jnp.bfloat16)
            if s == 0:
                return delta, upstream[:, :, 1:-1]
            back = back_conv(delta, flipped5)
            gradient = (upstream[:, :, 1:-1].astype(jnp.float32) + back).astype(jnp.bfloat16)
            return delta, gradient

        def backward_idle(upstream, pre_act):
            return jnp.zeros_like(upstream), jnp.zeros_like(upstream[:, :, 1:-1])

        delta, gradient = lax.cond(segment_no == s, backward_tick, backward_idle, upstream, pre_act)
        if s > 0:
            upstream = widened(gradient, segment_count, row_count, s, s - 1, 1)

        def grad_tick(x_ext, delta, grad_total):
            return kernel_grad(x_ext[:, :, 1:-1], delta[:, :, 1:-1]).reshape(27 * channels, channels)

        def grad_idle(x_ext, delta, grad_total):
            return grad_total

        grad_total = lax.cond(segment_no == s, grad_tick, grad_idle, x_ext, delta, grad_total)

    summed = tree_sum(grad_total, "rows", row_count, digits_of(row_count))
    return summed[None]


def solution(mesh):
    in_specs = (
        P(None, None, "rows", None, None),
        P("segment", None, None),
        P(None, None, "rows", None, None),
    )
    out_specs = P("segment", None, None)
    return jax.shard_map(
        per_device, mesh=mesh, in_specs=in_specs, out_specs=out_specs, check_vma=False
    )
```

```python
import jax
import jax.numpy as jnp
from jax import lax
from jax.sharding import PartitionSpec as P

AXES = ("segment", "rows")


def shifted(x, segment_count, row_count, seg_from, seg_to, row_step):
    pairs = []
    for i in range(row_count):
        j = i + row_step
        if 0 <= j < row_count:
            pairs.append((seg_from * row_count + i, seg_to * row_count + j))
    return lax.ppermute(x, AXES, pairs)


def widened(x, segment_count, row_count, seg_from, seg_to, width):
    rows = x.shape[2]
    if seg_from == seg_to:
        mid = x
    else:
        half = rows // 2
        mid = jnp.concatenate(
            [
                shifted(x[:, :, :half], segment_count, row_count, seg_from, seg_to, 0),
                shifted(x[:, :, half:], segment_count, row_count, seg_from, seg_to, 0),
            ],
            axis=2,
        )
    above = shifted(x[:, :, rows - width :], segment_count, row_count, seg_from, seg_to, 1)
    below = shifted(x[:, :, :width], segment_count, row_count, seg_from, seg_to, -1)
    return jnp.concatenate([above, mid, below], axis=2)


def forward_conv(x_ext, kernel5):
    return lax.conv_general_dilated(
        x_ext,
        kernel5,
        window_strides=(1, 1, 1),
        padding=((2, 0), (0, 0), (1, 1)),
        dimension_numbers=("NDHWC", "DHWIO", "NDHWC"),
        preferred_element_type=jnp.float32,
    )


def back_conv(delta_ext, flipped5):
    return lax.conv_general_dilated(
        delta_ext,
        flipped5,
        window_strides=(1, 1, 1),
        padding=((0, 2), (0, 0), (1, 1)),
        dimension_numbers=("NDHWC", "DHWIO", "NDHWC"),
        preferred_element_type=jnp.float32,
    )


def kernel_grad(x_ext, delta):
    padded = jnp.pad(x_ext, ((0, 0), (2, 0), (0, 0), (1, 1), (0, 0)))
    return lax.conv_general_dilated(
        padded,
        delta,
        window_strides=(1, 1, 1),
        padding="VALID",
        dimension_numbers=("CDHWN", "IDHWO", "DHWNC"),
        preferred_element_type=jnp.float32,
    )


def slope(pre_act):
    sigma = jax.nn.sigmoid(pre_act)
    return sigma * (1.0 + pre_act * (1.0 - sigma))


def pick(parts, index):
    out = parts[0]
    for k in range(1, len(parts)):
        out = jnp.where(index == k, parts[k], out)
    return out


def digit_pairs(count, stride, radix, step):
    pairs = []
    for j in range(count):
        digit = (j // stride) % radix
        pairs.append((j, j + ((digit + step) % radix - digit) * stride))
    return pairs


def tree_sum(x, axis, count, digits):
    index = lax.axis_index(axis)
    buf = x
    for stride, radix in digits:
        digit = (index // stride) % radix
        size = buf.shape[0] // radix
        parts = [buf[k * size : (k + 1) * size] for k in range(radix)]
        acc = pick(parts, digit)
        for step in range(1, radix):
            send = pick(parts, (digit + step) % radix).astype(jnp.bfloat16)
            got = lax.ppermute(send, axis, digit_pairs(count, stride, radix, step))
            acc = acc + got.astype(jnp.float32)
        buf = acc
    buf = buf.astype(jnp.bfloat16)
    for stride, radix in reversed(digits):
        digit = (index // stride) % radix
        gots = [buf]
        for step in range(1, radix):
            gots.append(lax.ppermute(buf, axis, digit_pairs(count, stride, radix, step)))
        buf = jnp.concatenate([pick(gots, (digit - k) % radix) for k in range(radix)])
    return buf.astype(jnp.float32)


def digits_of(count):
    if count == 64:
        return [(1, 2), (16, 4), (2, 2), (4, 4)]
    digits = []
    stride = 1
    while stride < count:
        digits.append((stride, 2))
        stride *= 2
    return digits


def per_device(clip, weights, cotangent):
    segment_count = lax.axis_size("segment")
    row_count = lax.axis_size("rows")
    segment_no = lax.axis_index("segment")
    channels = clip.shape[-1]
    kernel5 = weights[0].reshape(3, 3, 3, channels, channels)
    flipped5 = kernel5[::-1, ::-1, ::-1].transpose(0, 1, 2, 4, 3)

    rows = clip.shape[2]
    above = lax.ppermute(
        jnp.concatenate([clip[:, :, rows - 2 :], cotangent[:, :, rows - 1 :]], axis=2),
        "rows", [(i, i + 1) for i in range(row_count - 1)],
    )
    below = lax.ppermute(
        jnp.concatenate([clip[:, :, :2], cotangent[:, :, :1]], axis=2),
        "rows", [(i + 1, i) for i in range(row_count - 1)],
    )
    received = jnp.concatenate([above[:, :, :2], clip, below[:, :, :2]], axis=2)
    cot_ext = jnp.concatenate([above[:, :, 2:], cotangent, below[:, :, 2:]], axis=2)
    saved = []
    for s in range(segment_count):
        x_ext = received

        def forward_tick(x_ext):
            pre_act = forward_conv(x_ext, kernel5)
            core = x_ext[:, :, 2:-2].astype(jnp.float32)
            output = (core + jax.nn.silu(pre_act[:, :, 1:-1])).astype(jnp.bfloat16)
            return pre_act, output

        def forward_idle(x_ext):
            pre_act = jnp.zeros(x_ext.shape[:2] + (x_ext.shape[2] - 2,) + x_ext.shape[3:], jnp.float32)
            return pre_act, jnp.zeros_like(x_ext[:, :, 2:-2])

        pre_act, output = lax.cond(segment_no == s, forward_tick, forward_idle, x_ext)
        saved.append((x_ext, pre_act))
        if s + 1 < segment_count:
            received = widened(output, segment_count, row_count, s, s + 1, 2)

    last = segment_count - 1
    upstream = cot_ext
    grad_total = jnp.zeros((27 * channels, channels), jnp.float32)
    for s in reversed(range(segment_count)):
        x_ext, pre_act = saved[s]

        def backward_tick(upstream, pre_act):
            delta = (upstream.astype(jnp.float32) * slope(pre_act)).astype(jnp.bfloat16)
            if s == 0:
                return delta, upstream[:, :, 1:-1]
            back = back_conv(delta, flipped5)
            gradient = (upstream[:, :, 1:-1].astype(jnp.float32) + back).astype(jnp.bfloat16)
            return delta, gradient

        def backward_idle(upstream, pre_act):
            return jnp.zeros_like(upstream), jnp.zeros_like(upstream[:, :, 1:-1])

        delta, gradient = lax.cond(segment_no == s, backward_tick, backward_idle, upstream, pre_act)
        if s > 0:
            upstream = widened(gradient, segment_count, row_count, s, s - 1, 1)

        def grad_tick(x_ext, delta, grad_total):
            return kernel_grad(x_ext[:, :, 1:-1], delta[:, :, 1:-1]).reshape(27 * channels, channels)

        def grad_idle(x_ext, delta, grad_total):
            return grad_total

        grad_total = lax.cond(segment_no == s, grad_tick, grad_idle, x_ext, delta, grad_total)

    summed = tree_sum(grad_total, "rows", row_count, digits_of(row_count))
    return summed[None]


def solution(mesh):
    in_specs = (
        P(None, None, "rows", None, None),
        P("segment", None, None),
        P(None, None, "rows", None, None),
    )
    out_specs = P("segment", None, None)
    return jax.shard_map(
        per_device, mesh=mesh, in_specs=in_specs, out_specs=out_specs, check_vma=False
    )
```

```python
import jax
import jax.numpy as jnp
from jax import lax
from jax.sharding import PartitionSpec as P

AXES = ("segment", "rows")


def shifted(x, segment_count, row_count, seg_from, seg_to, row_step):
    pairs = []
    for i in range(row_count):
        j = i + row_step
        if 0 <= j < row_count:
            pairs.append((seg_from * row_count + i, seg_to * row_count + j))
    return lax.ppermute(x, AXES, pairs)


def handed(x, segment_count, row_count, seg_from, seg_to):
    half = x.shape[2] // 2
    return jnp.concatenate(
        [
            shifted(x[:, :, :half], segment_count, row_count, seg_from, seg_to, 0),
            shifted(x[:, :, half:], segment_count, row_count, seg_from, seg_to, 0),
        ],
        axis=2,
    )


def widened(x, segment_count, row_count, seg_from, seg_to, width):
    rows = x.shape[2]
    if seg_from == seg_to:
        mid = x
    else:
        mid = handed(x, segment_count, row_count, seg_from, seg_to)
    above = shifted(x[:, :, rows - width :], segment_count, row_count, seg_from, seg_to, 1)
    below = shifted(x[:, :, :width], segment_count, row_count, seg_from, seg_to, -1)
    return jnp.concatenate([above, mid, below], axis=2)


def forward_conv(x_ext, kernel5):
    return lax.conv_general_dilated(
        x_ext,
        kernel5,
        window_strides=(1, 1, 1),
        padding=((2, 0), (0, 0), (1, 1)),
        dimension_numbers=("NDHWC", "DHWIO", "NDHWC"),
        preferred_element_type=jnp.float32,
    )


def back_conv(delta_ext, flipped5):
    return lax.conv_general_dilated(
        delta_ext,
        flipped5,
        window_strides=(1, 1, 1),
        padding=((0, 2), (0, 0), (1, 1)),
        dimension_numbers=("NDHWC", "DHWIO", "NDHWC"),
        preferred_element_type=jnp.float32,
    )


def kernel_grad(x_ext, delta):
    padded = jnp.pad(x_ext, ((0, 0), (2, 0), (0, 0), (1, 1), (0, 0)))
    return lax.conv_general_dilated(
        padded,
        delta,
        window_strides=(1, 1, 1),
        padding="VALID",
        dimension_numbers=("CDHWN", "IDHWO", "DHWNC"),
        preferred_element_type=jnp.float32,
    )


def slope(pre_act):
    sigma = jax.nn.sigmoid(pre_act)
    return sigma * (1.0 + pre_act * (1.0 - sigma))


def pick(parts, index):
    out = parts[0]
    for k in range(1, len(parts)):
        out = jnp.where(index == k, parts[k], out)
    return out


def digit_pairs(count, stride, radix, step):
    pairs = []
    for j in range(count):
        digit = (j // stride) % radix
        pairs.append((j, j + ((digit + step) % radix - digit) * stride))
    return pairs


def tree_sum(x, axis, count, digits):
    index = lax.axis_index(axis)
    buf = x
    for stride, radix in digits:
        digit = (index // stride) % radix
        size = buf.shape[0] // radix
        parts = [buf[k * size : (k + 1) * size] for k in range(radix)]
        acc = pick(parts, digit)
        for step in range(1, radix):
            send = pick(parts, (digit + step) % radix).astype(jnp.bfloat16)
            got = lax.ppermute(send, axis, digit_pairs(count, stride, radix, step))
            acc = acc + got.astype(jnp.float32)
        buf = acc
    buf = buf.astype(jnp.bfloat16)
    for stride, radix in reversed(digits):
        digit = (index // stride) % radix
        gots = [buf]
        for step in range(1, radix):
            gots.append(lax.ppermute(buf, axis, digit_pairs(count, stride, radix, step)))
        buf = jnp.concatenate([pick(gots, (digit - k) % radix) for k in range(radix)])
    return buf.astype(jnp.float32)


def digits_of(count):
    if count == 64:
        return [(1, 2), (16, 4), (2, 2), (4, 4)]
    digits = []
    stride = 1
    while stride < count:
        digits.append((stride, 2))
        stride *= 2
    return digits


def per_device(clip, weights, cotangent):
    segment_count = lax.axis_size("segment")
    row_count = lax.axis_size("rows")
    segment_no = lax.axis_index("segment")
    channels = clip.shape[-1]
    kernel5 = weights[0].reshape(3, 3, 3, channels, channels)
    flipped5 = kernel5[::-1, ::-1, ::-1].transpose(0, 1, 2, 4, 3)

    rows = clip.shape[2]
    above = lax.ppermute(
        jnp.concatenate([clip[:, :, rows - 2 :], cotangent[:, :, rows - 1 :]], axis=2),
        "rows", [(i, i + 1) for i in range(row_count - 1)],
    )
    below = lax.ppermute(
        jnp.concatenate([clip[:, :, :2], cotangent[:, :, :1]], axis=2),
        "rows", [(i + 1, i) for i in range(row_count - 1)],
    )
    received = jnp.concatenate([above[:, :, :2], clip, below[:, :, :2]], axis=2)
    cot_ext = jnp.concatenate([above[:, :, 2:], cotangent, below[:, :, 2:]], axis=2)
    saved = []
    for s in range(segment_count):
        x_ext = received

        def forward_tick(x_ext):
            pre_act = forward_conv(x_ext, kernel5)
            core = x_ext[:, :, 2:-2].astype(jnp.float32)
            output = (core + jax.nn.silu(pre_act[:, :, 1:-1])).astype(jnp.bfloat16)
            return pre_act, output

        def forward_idle(x_ext):
            pre_act = jnp.zeros(x_ext.shape[:2] + (x_ext.shape[2] - 2,) + x_ext.shape[3:], jnp.float32)
            return pre_act, jnp.zeros_like(x_ext[:, :, 2:-2])

        pre_act, output = lax.cond(segment_no == s, forward_tick, forward_idle, x_ext)
        saved.append((x_ext, pre_act))
        if s + 1 < segment_count:
            received = widened(output, segment_count, row_count, s, s + 1, 2)

    last = segment_count - 1
    upstream = cot_ext
    grad_total = jnp.zeros((27 * channels, channels), jnp.float32)
    for s in reversed(range(segment_count)):
        x_ext, pre_act = saved[s]
        if s == 0:
            pre_act = pre_act[:, :, 1:-1]

        def backward_tick(upstream, pre_act):
            delta = (upstream.astype(jnp.float32) * slope(pre_act)).astype(jnp.bfloat16)
            if s == 0:
                return delta, upstream
            back = back_conv(delta, flipped5)
            gradient = (upstream[:, :, 1:-1].astype(jnp.float32) + back).astype(jnp.bfloat16)
            return delta, gradient

        def backward_idle(upstream, pre_act):
            if s == 0:
                return jnp.zeros_like(upstream), upstream
            return jnp.zeros_like(upstream), jnp.zeros_like(upstream[:, :, 1:-1])

        delta, gradient = lax.cond(segment_no == s, backward_tick, backward_idle, upstream, pre_act)
        if s > 1:
            upstream = widened(gradient, segment_count, row_count, s, s - 1, 1)
        elif s == 1:
            upstream = handed(gradient, segment_count, row_count, 1, 0)

        def grad_tick(x_ext, delta, grad_total):
            core = delta if s == 0 else delta[:, :, 1:-1]
            return kernel_grad(x_ext[:, :, 1:-1], core).reshape(27 * channels, channels)

        def grad_idle(x_ext, delta, grad_total):
            return grad_total

        grad_total = lax.cond(segment_no == s, grad_tick, grad_idle, x_ext, delta, grad_total)

    summed = tree_sum(grad_total, "rows", row_count, digits_of(row_count))
    return summed[None]


def solution(mesh):
    in_specs = (
        P(None, None, "rows", None, None),
        P("segment", None, None),
        P(None, None, "rows", None, None),
    )
    out_specs = P("segment", None, None)
    return jax.shard_map(
        per_device, mesh=mesh, in_specs=in_specs, out_specs=out_specs, check_vma=False
    )
```

```python
import jax
import jax.numpy as jnp
from jax import lax
from jax.sharding import PartitionSpec as P

AXES = ("segment", "rows")


def shifted(x, segment_count, row_count, seg_from, seg_to, row_step):
    pairs = []
    for i in range(row_count):
        j = i + row_step
        if 0 <= j < row_count:
            pairs.append((seg_from * row_count + i, seg_to * row_count + j))
    return lax.ppermute(x, AXES, pairs)


def handed(x, segment_count, row_count, seg_from, seg_to):
    half = x.shape[2] // 2
    return jnp.concatenate(
        [
            shifted(x[:, :, :half], segment_count, row_count, seg_from, seg_to, 0),
            shifted(x[:, :, half:], segment_count, row_count, seg_from, seg_to, 0),
        ],
        axis=2,
    )


def widened(x, segment_count, row_count, seg_from, seg_to, width):
    rows = x.shape[2]
    if seg_from == seg_to:
        mid = x
    else:
        mid = handed(x, segment_count, row_count, seg_from, seg_to)
    above = shifted(x[:, :, rows - width :], segment_count, row_count, seg_from, seg_to, 1)
    below = shifted(x[:, :, :width], segment_count, row_count, seg_from, seg_to, -1)
    return jnp.concatenate([above, mid, below], axis=2)


def forward_conv(x_ext, kernel5):
    return lax.conv_general_dilated(
        x_ext,
        kernel5,
        window_strides=(1, 1, 1),
        padding=((2, 0), (0, 0), (1, 1)),
        dimension_numbers=("NDHWC", "DHWIO", "NDHWC"),
        preferred_element_type=jnp.float32,
    )


def back_conv(delta_ext, flipped5):
    return lax.conv_general_dilated(
        delta_ext,
        flipped5,
        window_strides=(1, 1, 1),
        padding=((0, 2), (0, 0), (1, 1)),
        dimension_numbers=("NDHWC", "DHWIO", "NDHWC"),
        preferred_element_type=jnp.float32,
    )


def kernel_grad(x_ext, delta):
    padded = jnp.pad(x_ext, ((0, 0), (2, 0), (0, 0), (1, 1), (0, 0)))
    return lax.conv_general_dilated(
        padded,
        delta,
        window_strides=(1, 1, 1),
        padding="VALID",
        dimension_numbers=("CDHWN", "IDHWO", "DHWNC"),
        preferred_element_type=jnp.float32,
    )


def slope(pre_act):
    sigma = jax.nn.sigmoid(pre_act)
    return sigma * (1.0 + pre_act * (1.0 - sigma))


def pick(parts, index):
    out = parts[0]
    for k in range(1, len(parts)):
        out = jnp.where(index == k, parts[k], out)
    return out


def digit_pairs(count, stride, radix, step):
    pairs = []
    for j in range(count):
        digit = (j // stride) % radix
        pairs.append((j, j + ((digit + step) % radix - digit) * stride))
    return pairs


def tree_sum(x, axis, count, digits):
    index = lax.axis_index(axis)
    buf = x
    for stride, radix in digits:
        digit = (index // stride) % radix
        size = buf.shape[0] // radix
        parts = [buf[k * size : (k + 1) * size] for k in range(radix)]
        acc = pick(parts, digit)
        for step in range(1, radix):
            send = pick(parts, (digit + step) % radix).astype(jnp.bfloat16)
            got = lax.ppermute(send, axis, digit_pairs(count, stride, radix, step))
            acc = acc + got.astype(jnp.float32)
        buf = acc
    buf = buf.astype(jnp.bfloat16)
    for stride, radix in reversed(digits):
        digit = (index // stride) % radix
        gots = [buf]
        for step in range(1, radix):
            gots.append(lax.ppermute(buf, axis, digit_pairs(count, stride, radix, step)))
        buf = jnp.concatenate([pick(gots, (digit - k) % radix) for k in range(radix)])
    return buf.astype(jnp.float32)


def digits_of(count):
    if count == 64:
        return [(1, 2), (16, 4), (2, 2), (4, 4)]
    digits = []
    stride = 1
    while stride < count:
        digits.append((stride, 2))
        stride *= 2
    return digits


def per_device(clip, weights, cotangent):
    segment_count = lax.axis_size("segment")
    row_count = lax.axis_size("rows")
    segment_no = lax.axis_index("segment")
    channels = clip.shape[-1]
    kernel5 = weights[0].reshape(3, 3, 3, channels, channels)
    flipped5 = kernel5[::-1, ::-1, ::-1].transpose(0, 1, 2, 4, 3)

    rows = clip.shape[2]
    above = lax.ppermute(
        jnp.concatenate([clip[:, :, rows - 1 :], cotangent[:, :, rows - 1 :]], axis=2),
        "rows", [(i, i + 1) for i in range(row_count - 1)],
    )
    below = lax.ppermute(
        jnp.concatenate([clip[:, :, :1], cotangent[:, :, :1]], axis=2),
        "rows", [(i + 1, i) for i in range(row_count - 1)],
    )
    received = jnp.concatenate([above[:, :, :1], clip, below[:, :, :1]], axis=2)
    cot_ext = jnp.concatenate([above[:, :, 1:], cotangent, below[:, :, 1:]], axis=2)
    saved = []
    for s in range(segment_count):
        x_ext = received

        def forward_tick(x_ext):
            pre_act = forward_conv(x_ext, kernel5)
            if s == 0:
                core = x_ext[:, :, 1:-1].astype(jnp.float32)
                output = (core + jax.nn.silu(pre_act)).astype(jnp.bfloat16)
            else:
                core = x_ext[:, :, 2:-2].astype(jnp.float32)
                output = (core + jax.nn.silu(pre_act[:, :, 1:-1])).astype(jnp.bfloat16)
            return pre_act, output

        def forward_idle(x_ext):
            pre_act = jnp.zeros(x_ext.shape[:2] + (x_ext.shape[2] - 2,) + x_ext.shape[3:], jnp.float32)
            return pre_act, jnp.zeros_like(x_ext[:, :, 1 + (s > 0) : -1 - (s > 0)])

        pre_act, output = lax.cond(segment_no == s, forward_tick, forward_idle, x_ext)
        saved.append((x_ext, pre_act))
        if s + 1 < segment_count:
            received = widened(output, segment_count, row_count, s, s + 1, 2)

    last = segment_count - 1
    upstream = cot_ext
    grad_total = jnp.zeros((27 * channels, channels), jnp.float32)
    for s in reversed(range(segment_count)):
        x_ext, pre_act = saved[s]

        def backward_tick(upstream, pre_act):
            delta = (upstream.astype(jnp.float32) * slope(pre_act)).astype(jnp.bfloat16)
            if s == 0:
                return delta, upstream
            back = back_conv(delta, flipped5)
            gradient = (upstream[:, :, 1:-1].astype(jnp.float32) + back).astype(jnp.bfloat16)
            return delta, gradient

        def backward_idle(upstream, pre_act):
            if s == 0:
                return jnp.zeros_like(upstream), upstream
            return jnp.zeros_like(upstream), jnp.zeros_like(upstream[:, :, 1:-1])

        delta, gradient = lax.cond(segment_no == s, backward_tick, backward_idle, upstream, pre_act)
        if s > 1:
            upstream = widened(gradient, segment_count, row_count, s, s - 1, 1)
        elif s == 1:
            upstream = handed(gradient, segment_count, row_count, 1, 0)

        def grad_tick(x_ext, delta, grad_total):
            if s == 0:
                return kernel_grad(x_ext, delta).reshape(27 * channels, channels)
            return kernel_grad(x_ext[:, :, 1:-1], delta[:, :, 1:-1]).reshape(27 * channels, channels)

        def grad_idle(x_ext, delta, grad_total):
            return grad_total

        grad_total = lax.cond(segment_no == s, grad_tick, grad_idle, x_ext, delta, grad_total)

    summed = tree_sum(grad_total, "rows", row_count, digits_of(row_count))
    return summed[None]


def solution(mesh):
    in_specs = (
        P(None, None, "rows", None, None),
        P("segment", None, None),
        P(None, None, "rows", None, None),
    )
    out_specs = P("segment", None, None)
    return jax.shard_map(
        per_device, mesh=mesh, in_specs=in_specs, out_specs=out_specs, check_vma=False
    )
```

```python
import jax
import jax.numpy as jnp
from jax import lax
from jax.sharding import PartitionSpec as P

AXES = ("segment", "rows")


def shifted(x, segment_count, row_count, seg_from, seg_to, row_step):
    pairs = []
    for i in range(row_count):
        j = i + row_step
        if 0 <= j < row_count:
            pairs.append((seg_from * row_count + i, seg_to * row_count + j))
    return lax.ppermute(x, AXES, pairs)


def handed(x, segment_count, row_count, seg_from, seg_to):
    half = x.shape[2] // 2
    return jnp.concatenate(
        [
            shifted(x[:, :, :half], segment_count, row_count, seg_from, seg_to, 0),
            shifted(x[:, :, half:], segment_count, row_count, seg_from, seg_to, 0),
        ],
        axis=2,
    )


def widened(x, segment_count, row_count, seg_from, seg_to, width):
    rows = x.shape[2]
    if seg_from == seg_to:
        mid = x
    else:
        mid = handed(x, segment_count, row_count, seg_from, seg_to)
    above = shifted(x[:, :, rows - width :], segment_count, row_count, seg_from, seg_to, 1)
    below = shifted(x[:, :, :width], segment_count, row_count, seg_from, seg_to, -1)
    return jnp.concatenate([above, mid, below], axis=2)


def forward_conv(x_ext, kernel5):
    return lax.conv_general_dilated(
        x_ext,
        kernel5,
        window_strides=(1, 1, 1),
        padding=((2, 0), (0, 0), (1, 1)),
        dimension_numbers=("NDHWC", "DHWIO", "NDHWC"),
        preferred_element_type=jnp.float32,
    )


def back_conv(delta_ext, flipped5):
    return lax.conv_general_dilated(
        delta_ext,
        flipped5,
        window_strides=(1, 1, 1),
        padding=((0, 2), (0, 0), (1, 1)),
        dimension_numbers=("NDHWC", "DHWIO", "NDHWC"),
        preferred_element_type=jnp.float32,
    )


def kernel_grad(x_ext, delta):
    padded = jnp.pad(x_ext, ((0, 0), (2, 0), (0, 0), (1, 1), (0, 0)))
    return lax.conv_general_dilated(
        padded,
        delta,
        window_strides=(1, 1, 1),
        padding="VALID",
        dimension_numbers=("CDHWN", "IDHWO", "DHWNC"),
        preferred_element_type=jnp.float32,
    )


def slope(pre_act):
    sigma = jax.nn.sigmoid(pre_act)
    return sigma * (1.0 + pre_act * (1.0 - sigma))


def pick(parts, index):
    out = parts[0]
    for k in range(1, len(parts)):
        out = jnp.where(index == k, parts[k], out)
    return out


def digit_pairs(count, stride, radix, step):
    pairs = []
    for j in range(count):
        digit = (j // stride) % radix
        pairs.append((j, j + ((digit + step) % radix - digit) * stride))
    return pairs


def tree_sum(x, axis, count, digits):
    index = lax.axis_index(axis)
    buf = x
    for stride, radix in digits:
        digit = (index // stride) % radix
        size = buf.shape[0] // radix
        parts = [buf[k * size : (k + 1) * size] for k in range(radix)]
        acc = pick(parts, digit)
        for step in range(1, radix):
            send = pick(parts, (digit + step) % radix).astype(jnp.bfloat16)
            got = lax.ppermute(send, axis, digit_pairs(count, stride, radix, step))
            acc = acc + got.astype(jnp.float32)
        buf = acc
    buf = buf.astype(jnp.bfloat16)
    for stride, radix in reversed(digits):
        digit = (index // stride) % radix
        gots = [buf]
        for step in range(1, radix):
            gots.append(lax.ppermute(buf, axis, digit_pairs(count, stride, radix, step)))
        buf = jnp.concatenate([pick(gots, (digit - k) % radix) for k in range(radix)])
    return buf.astype(jnp.float32)


def digits_of(count):
    if count == 64:
        return [(1, 2), (16, 4), (2, 2), (4, 4)]
    digits = []
    stride = 1
    while stride < count:
        digits.append((stride, 2))
        stride *= 2
    return digits


def per_device(clip, weights, cotangent):
    segment_count = lax.axis_size("segment")
    row_count = lax.axis_size("rows")
    segment_no = lax.axis_index("segment")
    channels = clip.shape[-1]
    kernel5 = weights[0].reshape(3, 3, 3, channels, channels)
    flipped5 = kernel5[::-1, ::-1, ::-1].transpose(0, 1, 2, 4, 3)

    rows = clip.shape[2]
    above = lax.ppermute(
        jnp.concatenate([clip[:, :, rows - 1 :], cotangent[:, :, rows - 1 :]], axis=2),
        "rows", [(i, i + 1) for i in range(row_count - 1)],
    )
    below = lax.ppermute(
        jnp.concatenate([clip[:, :, :1], cotangent[:, :, :1]], axis=2),
        "rows", [(i + 1, i) for i in range(row_count - 1)],
    )
    received = jnp.concatenate([above[:, :, :1], clip, below[:, :, :1]], axis=2)
    cot_ext = jnp.concatenate([above[:, :, 1:], cotangent, below[:, :, 1:]], axis=2)
    saved = []
    for s in range(segment_count):
        x_ext = received

        def forward_tick(x_ext):
            pre_act = forward_conv(x_ext, kernel5)
            if s == 0:
                core = x_ext[:, :, 1:-1].astype(jnp.float32)
                output = (core + jax.nn.silu(pre_act)).astype(jnp.bfloat16)
            else:
                core = x_ext[:, :, 2:-2].astype(jnp.float32)
                output = (core + jax.nn.silu(pre_act[:, :, 1:-1])).astype(jnp.bfloat16)
            return slope(pre_act), output

        def forward_idle(x_ext):
            pre_act = jnp.zeros(x_ext.shape[:2] + (x_ext.shape[2] - 2,) + x_ext.shape[3:], jnp.float32)
            return pre_act, jnp.zeros_like(x_ext[:, :, 1 + (s > 0) : -1 - (s > 0)])

        pre_act, output = lax.cond(segment_no == s, forward_tick, forward_idle, x_ext)
        saved.append((x_ext, pre_act))
        if s + 1 < segment_count:
            received = widened(output, segment_count, row_count, s, s + 1, 2)

    last = segment_count - 1
    upstream = cot_ext
    grad_total = jnp.zeros((27 * channels, channels), jnp.float32)
    for s in reversed(range(segment_count)):
        x_ext, pre_act = saved[s]

        def backward_tick(upstream, pre_act):
            delta = (upstream.astype(jnp.float32) * pre_act).astype(jnp.bfloat16)
            if s == 0:
                return delta, upstream
            back = back_conv(delta, flipped5)
            gradient = (upstream[:, :, 1:-1].astype(jnp.float32) + back).astype(jnp.bfloat16)
            return delta, gradient

        def backward_idle(upstream, pre_act):
            if s == 0:
                return jnp.zeros_like(upstream), upstream
            return jnp.zeros_like(upstream), jnp.zeros_like(upstream[:, :, 1:-1])

        delta, gradient = lax.cond(segment_no == s, backward_tick, backward_idle, upstream, pre_act)
        if s > 1:
            upstream = widened(gradient, segment_count, row_count, s, s - 1, 1)
        elif s == 1:
            upstream = handed(gradient, segment_count, row_count, 1, 0)

        def grad_tick(x_ext, delta, grad_total):
            if s == 0:
                return kernel_grad(x_ext, delta).reshape(27 * channels, channels)
            return kernel_grad(x_ext[:, :, 1:-1], delta[:, :, 1:-1]).reshape(27 * channels, channels)

        def grad_idle(x_ext, delta, grad_total):
            return grad_total

        grad_total = lax.cond(segment_no == s, grad_tick, grad_idle, x_ext, delta, grad_total)

    summed = tree_sum(grad_total, "rows", row_count, digits_of(row_count))
    return summed[None]


def solution(mesh):
    in_specs = (
        P(None, None, "rows", None, None),
        P("segment", None, None),
        P(None, None, "rows", None, None),
    )
    out_specs = P("segment", None, None)
    return jax.shard_map(
        per_device, mesh=mesh, in_specs=in_specs, out_specs=out_specs, check_vma=False
    )
```

```python
import jax
import jax.numpy as jnp
from jax import lax
from jax.sharding import PartitionSpec as P

AXES = ("segment", "rows")


def shifted(x, segment_count, row_count, seg_from, seg_to, row_step):
    pairs = []
    for i in range(row_count):
        j = i + row_step
        if 0 <= j < row_count:
            pairs.append((seg_from * row_count + i, seg_to * row_count + j))
    return lax.ppermute(x, AXES, pairs)


def handed(x, segment_count, row_count, seg_from, seg_to):
    half = x.shape[2] // 2
    return jnp.concatenate(
        [
            shifted(x[:, :, :half], segment_count, row_count, seg_from, seg_to, 0),
            shifted(x[:, :, half:], segment_count, row_count, seg_from, seg_to, 0),
        ],
        axis=2,
    )


def widened(x, segment_count, row_count, seg_from, seg_to, width):
    rows = x.shape[2]
    if seg_from == seg_to:
        mid = x
    else:
        mid = handed(x, segment_count, row_count, seg_from, seg_to)
    above = shifted(x[:, :, rows - width :], segment_count, row_count, seg_from, seg_to, 1)
    below = shifted(x[:, :, :width], segment_count, row_count, seg_from, seg_to, -1)
    return jnp.concatenate([above, mid, below], axis=2)


def forward_conv(x_ext, kernel5):
    return lax.conv_general_dilated(
        x_ext,
        kernel5,
        window_strides=(1, 1, 1),
        padding=((2, 0), (0, 0), (1, 1)),
        dimension_numbers=("NDHWC", "DHWIO", "NDHWC"),
        preferred_element_type=jnp.float32,
    )


def back_conv(delta_ext, flipped5):
    return lax.conv_general_dilated(
        delta_ext,
        flipped5,
        window_strides=(1, 1, 1),
        padding=((0, 2), (0, 0), (1, 1)),
        dimension_numbers=("NDHWC", "DHWIO", "NDHWC"),
        preferred_element_type=jnp.float32,
    )


def kernel_grad(x_ext, delta):
    padded = jnp.pad(x_ext, ((0, 0), (2, 0), (0, 0), (1, 1), (0, 0)))
    return lax.conv_general_dilated(
        padded,
        delta,
        window_strides=(1, 1, 1),
        padding="VALID",
        dimension_numbers=("CDHWN", "IDHWO", "DHWNC"),
        preferred_element_type=jnp.float32,
    )


def slope(pre_act):
    sigma = jax.nn.sigmoid(pre_act)
    return sigma * (1.0 + pre_act * (1.0 - sigma))


def pick(parts, index):
    out = parts[0]
    for k in range(1, len(parts)):
        out = jnp.where(index == k, parts[k], out)
    return out


def digit_pairs(count, stride, radix, step):
    pairs = []
    for j in range(count):
        digit = (j // stride) % radix
        pairs.append((j, j + ((digit + step) % radix - digit) * stride))
    return pairs


def tree_sum(x, axis, count, digits):
    index = lax.axis_index(axis)
    buf = x
    for stride, radix in digits:
        digit = (index // stride) % radix
        size = buf.shape[0] // radix
        acc = lax.dynamic_slice_in_dim(buf, digit * size, size)
        for step in range(1, radix):
            part = lax.dynamic_slice_in_dim(buf, ((digit + step) % radix) * size, size)
            send = part.astype(jnp.bfloat16)
            got = lax.ppermute(send, axis, digit_pairs(count, stride, radix, step))
            acc = acc + got.astype(jnp.float32)
        buf = acc
    buf = buf.astype(jnp.bfloat16)
    for stride, radix in reversed(digits):
        digit = (index // stride) % radix
        size = buf.shape[0]
        out = jnp.zeros((radix * size,) + buf.shape[1:], buf.dtype)
        out = lax.dynamic_update_slice_in_dim(out, buf, digit * size, 0)
        for step in range(1, radix):
            got = lax.ppermute(buf, axis, digit_pairs(count, stride, radix, step))
            out = lax.dynamic_update_slice_in_dim(out, got, ((digit - step) % radix) * size, 0)
        buf = out
    return buf.astype(jnp.float32)


def digits_of(count):
    if count == 64:
        return [(1, 2), (16, 4), (2, 2), (4, 4)]
    digits = []
    stride = 1
    while stride < count:
        digits.append((stride, 2))
        stride *= 2
    return digits


def per_device(clip, weights, cotangent):
    segment_count = lax.axis_size("segment")
    row_count = lax.axis_size("rows")
    segment_no = lax.axis_index("segment")
    channels = clip.shape[-1]
    kernel5 = weights[0].reshape(3, 3, 3, channels, channels)
    flipped5 = kernel5[::-1, ::-1, ::-1].transpose(0, 1, 2, 4, 3)

    rows = clip.shape[2]
    above = lax.ppermute(
        jnp.concatenate([clip[:, :, rows - 1 :], cotangent[:, :, rows - 1 :]], axis=2),
        "rows", [(i, i + 1) for i in range(row_count - 1)],
    )
    below = lax.ppermute(
        jnp.concatenate([clip[:, :, :1], cotangent[:, :, :1]], axis=2),
        "rows", [(i + 1, i) for i in range(row_count - 1)],
    )
    received = jnp.concatenate([above[:, :, :1], clip, below[:, :, :1]], axis=2)
    cot_ext = jnp.concatenate([above[:, :, 1:], cotangent, below[:, :, 1:]], axis=2)
    saved = []
    for s in range(segment_count):
        x_ext = received

        def forward_tick(x_ext):
            pre_act = forward_conv(x_ext, kernel5)
            if s == 0:
                core = x_ext[:, :, 1:-1].astype(jnp.float32)
                output = (core + jax.nn.silu(pre_act)).astype(jnp.bfloat16)
            else:
                core = x_ext[:, :, 2:-2].astype(jnp.float32)
                output = (core + jax.nn.silu(pre_act[:, :, 1:-1])).astype(jnp.bfloat16)
            return slope(pre_act), output

        def forward_idle(x_ext):
            pre_act = jnp.zeros(x_ext.shape[:2] + (x_ext.shape[2] - 2,) + x_ext.shape[3:], jnp.float32)
            return pre_act, jnp.zeros_like(x_ext[:, :, 1 + (s > 0) : -1 - (s > 0)])

        pre_act, output = lax.cond(segment_no == s, forward_tick, forward_idle, x_ext)
        saved.append((x_ext, pre_act))
        if s + 1 < segment_count:
            received = widened(output, segment_count, row_count, s, s + 1, 2)

    last = segment_count - 1
    upstream = cot_ext
    grad_total = jnp.zeros((27 * channels, channels), jnp.float32)
    for s in reversed(range(segment_count)):
        x_ext, pre_act = saved[s]

        def backward_tick(upstream, pre_act):
            delta = (upstream.astype(jnp.float32) * pre_act).astype(jnp.bfloat16)
            if s == 0:
                return delta, upstream
            back = back_conv(delta, flipped5)
            gradient = (upstream[:, :, 1:-1].astype(jnp.float32) + back).astype(jnp.bfloat16)
            return delta, gradient

        def backward_idle(upstream, pre_act):
            if s == 0:
                return jnp.zeros_like(upstream), upstream
            return jnp.zeros_like(upstream), jnp.zeros_like(upstream[:, :, 1:-1])

        delta, gradient = lax.cond(segment_no == s, backward_tick, backward_idle, upstream, pre_act)
        if s > 1:
            upstream = widened(gradient, segment_count, row_count, s, s - 1, 1)
        elif s == 1:
            upstream = handed(gradient, segment_count, row_count, 1, 0)

        def grad_tick(x_ext, delta, grad_total):
            if s == 0:
                return kernel_grad(x_ext, delta).reshape(27 * channels, channels)
            return kernel_grad(x_ext[:, :, 1:-1], delta[:, :, 1:-1]).reshape(27 * channels, channels)

        def grad_idle(x_ext, delta, grad_total):
            return grad_total

        grad_total = lax.cond(segment_no == s, grad_tick, grad_idle, x_ext, delta, grad_total)

    summed = tree_sum(grad_total, "rows", row_count, digits_of(row_count))
    return summed[None]


def solution(mesh):
    in_specs = (
        P(None, None, "rows", None, None),
        P("segment", None, None),
        P(None, None, "rows", None, None),
    )
    out_specs = P("segment", None, None)
    return jax.shard_map(
        per_device, mesh=mesh, in_specs=in_specs, out_specs=out_specs, check_vma=False
    )
```

```python
import jax
import jax.numpy as jnp
from jax import lax
from jax.sharding import PartitionSpec as P

AXES = ("segment", "rows")


def shifted(x, segment_count, row_count, seg_from, seg_to, row_step):
    pairs = []
    for i in range(row_count):
        j = i + row_step
        if 0 <= j < row_count:
            pairs.append((seg_from * row_count + i, seg_to * row_count + j))
    return lax.ppermute(x, AXES, pairs)


def handed(x, segment_count, row_count, seg_from, seg_to):
    half = x.shape[2] // 2
    return jnp.concatenate(
        [
            shifted(x[:, :, :half], segment_count, row_count, seg_from, seg_to, 0),
            shifted(x[:, :, half:], segment_count, row_count, seg_from, seg_to, 0),
        ],
        axis=2,
    )


def widened(x, segment_count, row_count, seg_from, seg_to, width):
    rows = x.shape[2]
    if seg_from == seg_to:
        mid = x
    else:
        mid = handed(x, segment_count, row_count, seg_from, seg_to)
    above = shifted(x[:, :, rows - width :], segment_count, row_count, seg_from, seg_to, 1)
    below = shifted(x[:, :, :width], segment_count, row_count, seg_from, seg_to, -1)
    return jnp.concatenate([above, mid, below], axis=2)


def forward_conv(x_ext, kernel5):
    return lax.conv_general_dilated(
        x_ext,
        kernel5,
        window_strides=(1, 1, 1),
        padding=((2, 0), (0, 0), (1, 1)),
        dimension_numbers=("NDHWC", "DHWIO", "NDHWC"),
        preferred_element_type=jnp.float32,
    )


def back_conv(delta_ext, flipped5):
    return lax.conv_general_dilated(
        delta_ext,
        flipped5,
        window_strides=(1, 1, 1),
        padding=((0, 2), (0, 0), (1, 1)),
        dimension_numbers=("NDHWC", "DHWIO", "NDHWC"),
        preferred_element_type=jnp.float32,
    )


def kernel_grad(x_ext, delta):
    padded = jnp.pad(x_ext, ((0, 0), (2, 0), (0, 0), (1, 1), (0, 0)))
    return lax.conv_general_dilated(
        padded,
        delta,
        window_strides=(1, 1, 1),
        padding="VALID",
        dimension_numbers=("CDHWN", "IDHWO", "DHWNC"),
        preferred_element_type=jnp.float32,
    )


def slope(pre_act):
    sigma = jax.nn.sigmoid(pre_act)
    return sigma * (1.0 + pre_act * (1.0 - sigma))


def pick(parts, index):
    out = parts[0]
    for k in range(1, len(parts)):
        out = jnp.where(index == k, parts[k], out)
    return out


def digit_pairs(count, stride, radix, step):
    pairs = []
    for j in range(count):
        digit = (j // stride) % radix
        pairs.append((j, j + ((digit + step) % radix - digit) * stride))
    return pairs


def tree_sum(x, axis, count, digits):
    index = lax.axis_index(axis)
    buf = x
    for stride, radix in digits:
        digit = (index // stride) % radix
        size = buf.shape[0] // radix
        acc = lax.dynamic_slice_in_dim(buf, digit * size, size)
        for step in range(1, radix):
            part = lax.dynamic_slice_in_dim(buf, ((digit + step) % radix) * size, size)
            send = part.astype(jnp.bfloat16)
            got = lax.ppermute(send, axis, digit_pairs(count, stride, radix, step))
            acc = acc + got.astype(jnp.float32)
        buf = acc
    buf = buf.astype(jnp.bfloat16)
    for level, (stride, radix) in reversed(list(enumerate(digits))):
        digit = (index // stride) % radix
        size = buf.shape[0]
        kind = jnp.float32 if level == 0 else buf.dtype
        out = jnp.zeros((radix * size,) + buf.shape[1:], kind)
        out = lax.dynamic_update_slice_in_dim(out, buf.astype(kind), digit * size, 0)
        for step in range(1, radix):
            got = lax.ppermute(buf, axis, digit_pairs(count, stride, radix, step))
            out = lax.dynamic_update_slice_in_dim(out, got.astype(kind), ((digit - step) % radix) * size, 0)
        buf = out
    return buf.astype(jnp.float32)


def digits_of(count):
    if count == 64:
        return [(1, 2), (16, 4), (2, 2), (4, 4)]
    digits = []
    stride = 1
    while stride < count:
        digits.append((stride, 2))
        stride *= 2
    return digits


def per_device(clip, weights, cotangent):
    segment_count = lax.axis_size("segment")
    row_count = lax.axis_size("rows")
    segment_no = lax.axis_index("segment")
    channels = clip.shape[-1]
    kernel5 = weights[0].reshape(3, 3, 3, channels, channels)
    flipped5 = kernel5[::-1, ::-1, ::-1].transpose(0, 1, 2, 4, 3)

    rows = clip.shape[2]
    above = lax.ppermute(
        jnp.concatenate([clip[:, :, rows - 1 :], cotangent[:, :, rows - 1 :]], axis=2),
        "rows", [(i, i + 1) for i in range(row_count - 1)],
    )
    below = lax.ppermute(
        jnp.concatenate([clip[:, :, :1], cotangent[:, :, :1]], axis=2),
        "rows", [(i + 1, i) for i in range(row_count - 1)],
    )
    received = jnp.concatenate([above[:, :, :1], clip, below[:, :, :1]], axis=2)
    cot_ext = jnp.concatenate([above[:, :, 1:], cotangent, below[:, :, 1:]], axis=2)
    saved = []
    for s in range(segment_count):
        x_ext = received

        def forward_tick(x_ext):
            pre_act = forward_conv(x_ext, kernel5)
            if s == 0:
                core = x_ext[:, :, 1:-1].astype(jnp.float32)
                output = (core + jax.nn.silu(pre_act)).astype(jnp.bfloat16)
            else:
                core = x_ext[:, :, 2:-2].astype(jnp.float32)
                output = (core + jax.nn.silu(pre_act[:, :, 1:-1])).astype(jnp.bfloat16)
            return slope(pre_act), output

        def forward_idle(x_ext):
            pre_act = jnp.zeros(x_ext.shape[:2] + (x_ext.shape[2] - 2,) + x_ext.shape[3:], jnp.float32)
            return pre_act, jnp.zeros_like(x_ext[:, :, 1 + (s > 0) : -1 - (s > 0)])

        pre_act, output = lax.cond(segment_no == s, forward_tick, forward_idle, x_ext)
        saved.append((x_ext, pre_act))
        if s + 1 < segment_count:
            received = widened(output, segment_count, row_count, s, s + 1, 2)

    last = segment_count - 1
    upstream = cot_ext
    grad_total = jnp.zeros((27 * channels, channels), jnp.float32)
    for s in reversed(range(segment_count)):
        x_ext, pre_act = saved[s]

        def backward_tick(upstream, pre_act):
            delta = (upstream.astype(jnp.float32) * pre_act).astype(jnp.bfloat16)
            if s == 0:
                return delta, upstream
            back = back_conv(delta, flipped5)
            gradient = (upstream[:, :, 1:-1].astype(jnp.float32) + back).astype(jnp.bfloat16)
            return delta, gradient

        def backward_idle(upstream, pre_act):
            if s == 0:
                return jnp.zeros_like(upstream), upstream
            return jnp.zeros_like(upstream), jnp.zeros_like(upstream[:, :, 1:-1])

        delta, gradient = lax.cond(segment_no == s, backward_tick, backward_idle, upstream, pre_act)
        if s > 1:
            upstream = widened(gradient, segment_count, row_count, s, s - 1, 1)
        elif s == 1:
            upstream = handed(gradient, segment_count, row_count, 1, 0)

        def grad_tick(x_ext, delta, grad_total):
            if s == 0:
                return kernel_grad(x_ext, delta).reshape(27 * channels, channels)
            return kernel_grad(x_ext[:, :, 1:-1], delta[:, :, 1:-1]).reshape(27 * channels, channels)

        def grad_idle(x_ext, delta, grad_total):
            return grad_total

        grad_total = lax.cond(segment_no == s, grad_tick, grad_idle, x_ext, delta, grad_total)

    summed = tree_sum(grad_total, "rows", row_count, digits_of(row_count))
    return summed[None]


def solution(mesh):
    in_specs = (
        P(None, None, "rows", None, None),
        P("segment", None, None),
        P(None, None, "rows", None, None),
    )
    out_specs = P("segment", None, None)
    return jax.shard_map(
        per_device, mesh=mesh, in_specs=in_specs, out_specs=out_specs, check_vma=False
    )
```
